256 devices in a mesh: dp: 4 (over z_lo, core), cp: 16 (over y, z_hi), tp: 4 (over x).
Axes of the slice: x: 4, y: 4, z: 8 (z_hi: 4, z_lo: 2; z = z_hi * 2 + z_lo), core: 2. Of those that a mesh axis runs over, the one named last changes fastest.
Arguments:
- hidden: bfloat16 [4, 2048, 8192], P('dp', 'cp'), may hold values from -6 to 6
- query: bfloat16 [4, 2048, 8192], P('dp', 'cp', 'tp'), may hold values from -360 to 360
- grad_out: bfloat16 [4, 2048, 8192], P('dp', 'cp', 'tp'), may hold values from -6 to 6
- k_weight: bfloat16 [8192, 1024], P('dp', 'tp'), may hold values from -0.0625 to 0.0625
- v_weight: bfloat16 [8192, 1024], P('dp', 'tp'), may hold values from -0.0625 to 0.0625
- doc_starts: int32 [4, 4], P('dp'), may hold values from 0 to 2047, as said below
Outputs:
- attn_out: bfloat16 [4, 2048, 8192], P('dp', 'cp', 'tp')
- query_grad: bfloat16 [4, 2048, 8192], P('dp', 'cp', 'tp')
- k_weight_grad: float32 [8192, 1024], P(('dp', 'cp'), 'tp')
- v_weight_grad: float32 [8192, 1024], P(('dp', 'cp'), 'tp')
The draws below stay inside these ranges and needn't reach their ends.
Inputs may be any that keep to these rules, and one draw needn't show every extreme that they name: `doc_starts`: in each sequence the starts strictly increase and the first is 0.
All inputs are finite; a program needn't handle non-finite values.
Results may differ from the reference program's by a relative error of at most 0.04.
The reference program's roundings to bfloat16 on the way count: a program that leaves them out, or rounds other values in their place, can miss the bound.
Values may be sent and summed in bfloat16 or wider, within the bound.
No kernel may reach another device: no remote copies, remote signals or barrier semaphores. Data moves between devices by JAX's collectives and lax.ppermute only.
A program may use at most 128 MiB of HBM per device.

```python
import jax
import jax.numpy as jnp
from jax import lax

D = 8192
HQ = 64
HK = 8
DH = 128
TOK_DEV = 128
DOCS = 4
SEQ = 2048
N_DP = 4


def draw_doc_starts(key, part):
    split_keys = jax.random.split(key, N_DP + 1)
    keys_all = split_keys[:N_DP]
    chosen = jax.random.randint(split_keys[N_DP], (), 0, N_DP)
    flags = jnp.arange(N_DP, dtype=jnp.int32) == chosen

    def one_group(group_key, flag):
        cuts = jax.random.permutation(group_key, SEQ - 1)[:DOCS - 1] + 1
        cuts = jnp.sort(cuts.astype(jnp.int32))
        last_cut = jnp.where(flag, jnp.int32(SEQ - 1), cuts[DOCS - 2])
        cuts = cuts.at[DOCS - 2].set(last_cut)
        return jnp.concatenate([jnp.zeros((1,), jnp.int32), cuts])
    return jax.vmap(one_group)(keys_all, flags)


def draw_query(key, part):
    first = jax.random.fold_in(key, 0)
    shape_all = (N_DP, SEQ, HQ * DH)
    base = jnp.clip(jax.random.normal(first, shape_all, jnp.float32), -4.0, 4.0)
    return base.astype(jnp.bfloat16)


def levels(rng, dims, shards, low, top_value):
    loudness, own = 1.0, jax.random.fold_in(rng, 6)
    for position, parts in shards:
        heights = jnp.exp(jax.random.uniform(jax.random.fold_in(own, position), (parts,), jnp.float32, low / len(shards), top_value / len(shards)))
        loudness = loudness * jnp.repeat(heights, dims[position] // parts).reshape([-1 if axis == position else 1 for axis in range(len(dims))])
    return loudness


def normal_values(stream_key, extent, width, limit, pieces=(), held_as=jnp.bfloat16):
    gain = levels(stream_key, extent, pieces, -0.22, 0.18) if pieces else 1.0
    array = jax.random.normal(stream_key, extent, jnp.float32) * width * gain
    return jnp.minimum(jnp.maximum(array, -limit), limit).astype(held_as)


def setup_inputs(seed: int = 0) -> dict:
    key_of = jax.random.split(jax.random.key(seed), 7)
    hidden = normal_values(key_of[0], (N_DP, SEQ, D), 1.0, 6.0, ((0, 4), (1, 16)))
    query = draw_query(jax.random.fold_in(key_of[6], 71), 0)
    grad_out = normal_values(key_of[2], (N_DP, SEQ, HQ * DH), 1.0, 6.0, ((0, 4), (1, 16), (2, 4)))
    k_weight = normal_values(key_of[3], (D, HK * DH), D ** -0.5, 0.0625, ((0, 4), (1, 4)))
    v_weight = normal_values(key_of[4], (D, HK * DH), D ** -0.5, 0.0625, ((0, 4), (1, 4)))
    doc_starts = draw_doc_starts(jax.random.fold_in(key_of[6], 71), 0)
    return dict(hidden=hidden, query=query, grad_out=grad_out, k_weight=k_weight, v_weight=v_weight, doc_starts=doc_starts)


NEG_BIG = -1e30


def place(rows, tok_rows, seq_rows):
    stretch = rows // tok_rows
    within = rows % tok_rows
    half_rows = tok_rows // 2
    return jnp.where(within < half_rows, stretch * half_rows + within,
                     seq_rows - (stretch + 1) * half_rows + within - half_rows)


def doc_index(positions, starts):
    return jnp.sum((starts[None, :] <= positions[:, None]).astype(jnp.int32), axis=1) - 1


def reference(hidden, query, grad_out, k_weight, v_weight, doc_starts):
    score_scale = DH ** -0.5
    per_group = HQ // HK
    places = place(jnp.arange(SEQ, dtype=jnp.int32), TOK_DEV, SEQ)
    outputs = []
    query_grads = []
    k_total = jnp.zeros((D, HK * DH), jnp.float32)
    v_total = jnp.zeros((D, HK * DH), jnp.float32)
    for group_index in range(N_DP):
        inputs = hidden[group_index]
        keys = jnp.dot(inputs, k_weight, preferred_element_type=jnp.float32).astype(jnp.bfloat16)
        values = jnp.dot(inputs, v_weight, preferred_element_type=jnp.float32).astype(jnp.bfloat16)
        docs = doc_index(places, doc_starts[group_index])
        allowed = (places[None, :] <= places[:, None]) & (docs[None, :] == docs[:, None])
        queries = query[group_index].reshape(SEQ, HK, per_group, DH).transpose(1, 0, 2, 3)
        upstream = grad_out[group_index].reshape(SEQ, HK, per_group, DH).transpose(1, 0, 2, 3)
        key_heads = keys.reshape(SEQ, HK, DH).transpose(1, 0, 2)
        value_heads = values.reshape(SEQ, HK, DH).transpose(1, 0, 2)

        def one_head(operands):
            head_q, head_k, head_v, head_up = operands
            scores = jnp.einsum('qid,kd->iqk', head_q.astype(jnp.float32), head_k.astype(jnp.float32)) * score_scale
            scores = jnp.where(allowed[None], scores, NEG_BIG)
            top_score = jnp.max(scores, axis=-1)
            expos = jnp.where(allowed[None], jnp.exp(scores - top_score[..., None]), 0.0)
            log_total = top_score + jnp.log(jnp.sum(expos, axis=-1))
            weights = jnp.where(allowed[None], jnp.exp(scores - log_total[..., None]), 0.0)
            weights_bf = weights.astype(jnp.bfloat16)
            head_out = jnp.einsum('iqk,kd->qid', weights_bf.astype(jnp.float32),
                                  head_v.astype(jnp.float32)).astype(jnp.bfloat16)
            delta = jnp.einsum('qid,qid->iq', head_up.astype(jnp.float32), head_out.astype(jnp.float32))
            prob_grads = jnp.einsum('qid,kd->iqk', head_up.astype(jnp.float32), head_v.astype(jnp.float32))
            score_grads = (weights * (prob_grads - delta[..., None])).astype(jnp.bfloat16)
            head_qgrad = (jnp.einsum('iqk,kd->qid', score_grads.astype(jnp.float32),
                                     head_k.astype(jnp.float32)) * score_scale).astype(jnp.bfloat16)
            head_kgrad = jnp.einsum('iqk,qid->kd', score_grads.astype(jnp.float32),
                                    head_q.astype(jnp.float32)) * score_scale
            head_vgrad = jnp.einsum('iqk,qid->kd', weights_bf.astype(jnp.float32),
                                    head_up.astype(jnp.float32))
            return head_out, head_qgrad, head_kgrad, head_vgrad

        head_out, head_qgrad, head_kgrad, head_vgrad = lax.map(one_head, (queries, key_heads, value_heads, upstream))
        outputs.append(head_out.transpose(1, 0, 2, 3).reshape(SEQ, HQ * DH))
        query_grads.append(head_qgrad.transpose(1, 0, 2, 3).reshape(SEQ, HQ * DH))
        key_grad = head_kgrad.transpose(1, 0, 2).reshape(SEQ, HK * DH).astype(jnp.bfloat16)
        value_grad = head_vgrad.transpose(1, 0, 2).reshape(SEQ, HK * DH).astype(jnp.bfloat16)
        k_total = k_total + jnp.dot(inputs.T, key_grad, preferred_element_type=jnp.float32)
        v_total = v_total + jnp.dot(inputs.T, value_grad, preferred_element_type=jnp.float32)
    return jnp.stack(outputs), jnp.stack(query_grads), k_total, v_total
```

```python
import jax
import jax.numpy as jnp
from jax import lax
from jax.sharding import PartitionSpec as P

DH = 128


NEG_BIG = -1e30


def place(rows, tok_rows, seq_rows):
    stretch = rows // tok_rows
    within = rows % tok_rows
    half_rows = tok_rows // 2
    return jnp.where(
        within < half_rows,
        stretch * half_rows + within,
        seq_rows - (stretch + 1) * half_rows + within - half_rows,
    )


def doc_index(positions, starts):
    return jnp.sum((starts[None, :] <= positions[:, None]).astype(jnp.int32), axis=1) - 1


def on_device(hidden, query, grad_out, k_weight, v_weight, doc_starts):
    inputs = hidden[0]
    tok_rows, width = inputs.shape
    cp_count = lax.axis_size("cp")
    dp_count = lax.axis_size("dp")
    seq_rows = tok_rows * cp_count
    score_scale = DH ** (-0.5)
    kv_width = k_weight.shape[1]
    kv_heads = kv_width // DH
    per_group = query.shape[2] // DH // kv_heads
    starts = doc_starts[0]

    blk = width // (dp_count * cp_count)
    cols = inputs.reshape(tok_rows, dp_count, cp_count, blk).transpose(2, 0, 1, 3)
    cols = lax.all_to_all(cols, "cp", 0, 0, tiled=True)

    both_w = jnp.concatenate([k_weight, v_weight], axis=1)
    both_w = lax.all_gather(both_w, "dp", axis=0, tiled=True)
    kv = jnp.dot(inputs, both_w, preferred_element_type=jnp.float32).astype(jnp.bfloat16)
    kv_all = lax.all_gather(kv, "cp", axis=0, tiled=True)
    key_heads = kv_all[:, :kv_width].reshape(seq_rows, kv_heads, DH)
    value_heads = kv_all[:, kv_width:].reshape(seq_rows, kv_heads, DH)

    own_rows = lax.axis_index("cp") * tok_rows + jnp.arange(tok_rows, dtype=jnp.int32)
    own_place = place(own_rows, tok_rows, seq_rows)
    own_doc = doc_index(own_place, starts)
    key_place = place(jnp.arange(seq_rows, dtype=jnp.int32), tok_rows, seq_rows)
    key_doc = doc_index(key_place, starts)
    allowed = (key_place[None, :] <= own_place[:, None]) & (key_doc[None, :] == own_doc[:, None])

    queries = query[0].reshape(tok_rows, kv_heads, per_group, DH)
    upstream = grad_out[0].reshape(tok_rows, kv_heads, per_group, DH)

    scores = (
        jnp.einsum("qgid,kgd->giqk", queries, key_heads, preferred_element_type=jnp.float32)
        * score_scale
    )
    scores = jnp.where(allowed, scores, NEG_BIG)
    top_score = jnp.max(scores, axis=-1)
    expos = jnp.where(allowed, jnp.exp(scores - top_score[..., None]), 0.0)
    log_total = top_score + jnp.log(jnp.sum(expos, axis=-1))
    weights = jnp.where(allowed, jnp.exp(scores - log_total[..., None]), 0.0)
    weights_bf = weights.astype(jnp.bfloat16)
    out_rows = jnp.einsum(
        "giqk,kgd->qgid", weights_bf, value_heads, preferred_element_type=jnp.float32
    ).astype(jnp.bfloat16)
    delta = jnp.transpose(
        jnp.sum(upstream.astype(jnp.float32) * out_rows.astype(jnp.float32), axis=-1), (1, 2, 0)
    )
    prob_grads = jnp.einsum(
        "qgid,kgd->giqk", upstream, value_heads, preferred_element_type=jnp.float32
    )
    score_grads = (weights * (prob_grads - delta[..., None])).astype(jnp.bfloat16)
    query_acc = (
        jnp.einsum("giqk,kgd->qgid", score_grads, key_heads, preferred_element_type=jnp.float32)
        * score_scale
    )
    key_term = (
        jnp.einsum("giqk,qgid->kgd", score_grads, queries, preferred_element_type=jnp.float32)
        * score_scale
    )
    value_term = jnp.einsum(
        "giqk,qgid->kgd", weights_bf, upstream, preferred_element_type=jnp.float32
    )
    both_terms = jnp.concatenate(
        [key_term.reshape(seq_rows, kv_width), value_term.reshape(seq_rows, kv_width)], axis=1
    ).astype(jnp.bfloat16)
    both_grads = lax.psum(both_terms, "cp")

    grads = both_grads.reshape(cp_count, tok_rows, 2 * kv_width)
    partial = jnp.einsum("ctjb,ctn->jbn", cols, grads, preferred_element_type=jnp.float32)
    result = lax.psum_scatter(partial, "dp", scatter_dimension=0, tiled=True)[0]

    attn_rows = out_rows.reshape(1, tok_rows, kv_heads * per_group * DH)
    query_rows = query_acc.astype(jnp.bfloat16).reshape(1, tok_rows, kv_heads * per_group * DH)
    return (attn_rows, query_rows, result[:, :kv_width], result[:, kv_width:])


def solution(mesh):
    placed = (
        P("dp", "cp", None),
        P("dp", "cp", "tp"),
        P("dp", "cp", "tp"),
        P("dp", "tp"),
        P("dp", "tp"),
        P("dp", None),
    )
    return jax.shard_map(
        on_device,
        mesh=mesh,
        in_specs=placed,
        out_specs=(
            P("dp", "cp", "tp"),
            P("dp", "cp", "tp"),
            P(("dp", "cp"), "tp"),
            P(("dp", "cp"), "tp"),
        ),
        check_vma=False,
    )
```

```python
import jax
import jax.numpy as jnp
from jax import lax
from jax.sharding import PartitionSpec as P

DH = 128


NEG_BIG = -1e30


def place(rows, tok_rows, seq_rows):
    stretch = rows // tok_rows
    within = rows % tok_rows
    half_rows = tok_rows // 2
    return jnp.where(
        within < half_rows,
        stretch * half_rows + within,
        seq_rows - (stretch + 1) * half_rows + within - half_rows,
    )


def doc_index(positions, starts):
    return jnp.sum((starts[None, :] <= positions[:, None]).astype(jnp.int32), axis=1) - 1


def gather_over(piece, axis, count):
    spread = jnp.broadcast_to(piece[None], (count,) + piece.shape)
    return lax.all_to_all(spread, axis, 0, 0, tiled=True)


def reduce_over(blocks, axis):
    received = lax.all_to_all(blocks, axis, 0, 0, tiled=True)
    return jnp.sum(received.astype(jnp.float32), axis=0)


def on_device(hidden, query, grad_out, k_weight, v_weight, doc_starts):
    inputs = hidden[0]
    tok_rows, width = inputs.shape
    cp_count = lax.axis_size("cp")
    dp_count = lax.axis_size("dp")
    seq_rows = tok_rows * cp_count
    score_scale = DH ** (-0.5)
    kv_width = k_weight.shape[1]
    kv_heads = kv_width // DH
    per_group = query.shape[2] // DH // kv_heads
    starts = doc_starts[0]

    blk = width // (dp_count * cp_count)
    cols = inputs.reshape(tok_rows, dp_count, cp_count, blk).transpose(2, 0, 1, 3)
    cols = lax.all_to_all(cols, "cp", 0, 0, tiled=True)

    both_w = jnp.concatenate([k_weight, v_weight], axis=1)
    w_rows = both_w.shape[0]
    by_dp = inputs.reshape(tok_rows, dp_count, w_rows).transpose(1, 0, 2)
    by_dp = lax.all_to_all(by_dp, "dp", 0, 0, tiled=True)
    kv_part = jnp.einsum("str,rn->stn", by_dp, both_w, preferred_element_type=jnp.float32)
    kv = reduce_over(kv_part, "dp").astype(jnp.bfloat16)
    kv_all = gather_over(kv, "cp", cp_count).reshape(seq_rows, 2 * kv_width)
    key_heads = kv_all[:, :kv_width].reshape(seq_rows, kv_heads, DH)
    value_heads = kv_all[:, kv_width:].reshape(seq_rows, kv_heads, DH)

    own_rows = lax.axis_index("cp") * tok_rows + jnp.arange(tok_rows, dtype=jnp.int32)
    own_place = place(own_rows, tok_rows, seq_rows)
    own_doc = doc_index(own_place, starts)
    key_place = place(jnp.arange(seq_rows, dtype=jnp.int32), tok_rows, seq_rows)
    key_doc = doc_index(key_place, starts)
    allowed = (key_place[None, :] <= own_place[:, None]) & (key_doc[None, :] == own_doc[:, None])

    queries = query[0].reshape(tok_rows, kv_heads, per_group, DH)
    upstream = grad_out[0].reshape(tok_rows, kv_heads, per_group, DH)

    scores = (
        jnp.einsum("qgid,kgd->giqk", queries, key_heads, preferred_element_type=jnp.float32)
        * score_scale
    )
    scores = jnp.where(allowed, scores, NEG_BIG)
    top_score = jnp.max(scores, axis=-1)
    expos = jnp.where(allowed, jnp.exp(scores - top_score[..., None]), 0.0)
    log_total = top_score + jnp.log(jnp.sum(expos, axis=-1))
    weights = jnp.where(allowed, jnp.exp(scores - log_total[..., None]), 0.0)
    weights_bf = weights.astype(jnp.bfloat16)
    out_rows = jnp.einsum(
        "giqk,kgd->qgid", weights_bf, value_heads, preferred_element_type=jnp.float32
    ).astype(jnp.bfloat16)
    delta = jnp.transpose(
        jnp.sum(upstream.astype(jnp.float32) * out_rows.astype(jnp.float32), axis=-1), (1, 2, 0)
    )
    prob_grads = jnp.einsum(
        "qgid,kgd->giqk", upstream, value_heads, preferred_element_type=jnp.float32
    )
    score_grads = (weights * (prob_grads - delta[..., None])).astype(jnp.bfloat16)
    query_acc = (
        jnp.einsum("giqk,kgd->qgid", score_grads, key_heads, preferred_element_type=jnp.float32)
        * score_scale
    )
    key_term = (
        jnp.einsum("giqk,qgid->kgd", score_grads, queries, preferred_element_type=jnp.float32)
        * score_scale
    )
    value_term = jnp.einsum(
        "giqk,qgid->kgd", weights_bf, upstream, preferred_element_type=jnp.float32
    )
    both_terms = jnp.concatenate(
        [key_term.reshape(seq_rows, kv_width), value_term.reshape(seq_rows, kv_width)], axis=1
    ).astype(jnp.bfloat16)
    own_grads = reduce_over(both_terms.reshape(cp_count, tok_rows, 2 * kv_width), "cp")
    grads = gather_over(own_grads.astype(jnp.bfloat16), "cp", cp_count)

    partial = jnp.einsum("ctjb,ctn->jbn", cols, grads, preferred_element_type=jnp.float32)
    result = reduce_over(partial, "dp")

    attn_rows = out_rows.reshape(1, tok_rows, kv_heads * per_group * DH)
    query_rows = query_acc.astype(jnp.bfloat16).reshape(1, tok_rows, kv_heads * per_group * DH)
    return (attn_rows, query_rows, result[:, :kv_width], result[:, kv_width:])


def solution(mesh):
    placed = (
        P("dp", "cp", None),
        P("dp", "cp", "tp"),
        P("dp", "cp", "tp"),
        P("dp", "tp"),
        P("dp", "tp"),
        P("dp", None),
    )
    return jax.shard_map(
        on_device,
        mesh=mesh,
        in_specs=placed,
        out_specs=(
            P("dp", "cp", "tp"),
            P("dp", "cp", "tp"),
            P(("dp", "cp"), "tp"),
            P(("dp", "cp"), "tp"),
        ),
        check_vma=False,
    )
```

```python
import jax
import jax.numpy as jnp
from jax import lax
from jax.sharding import PartitionSpec as P

DH = 128


NEG_BIG = -1e30


def place(rows, tok_rows, seq_rows):
    stretch = rows // tok_rows
    within = rows % tok_rows
    half_rows = tok_rows // 2
    return jnp.where(
        within < half_rows,
        stretch * half_rows + within,
        seq_rows - (stretch + 1) * half_rows + within - half_rows,
    )


def doc_index(positions, starts):
    return jnp.sum((starts[None, :] <= positions[:, None]).astype(jnp.int32), axis=1) - 1


def gather_over(piece, axis, count):
    spread = jnp.broadcast_to(piece[None], (count,) + piece.shape)
    return lax.all_to_all(spread, axis, 0, 0, tiled=True)


def reduce_over(blocks, axis):
    received = lax.all_to_all(blocks, axis, 0, 0, tiled=True)
    return jnp.sum(received.astype(jnp.float32), axis=0)


def on_device(hidden, query, grad_out, k_weight, v_weight, doc_starts):
    inputs = hidden[0]
    tok_rows, width = inputs.shape
    cp_count = lax.axis_size("cp")
    dp_count = lax.axis_size("dp")
    seq_rows = tok_rows * cp_count
    score_scale = DH ** (-0.5)
    kv_width = k_weight.shape[1]
    kv_heads = kv_width // DH
    per_group = query.shape[2] // DH // kv_heads
    starts = doc_starts[0]

    blk = width // (dp_count * cp_count)
    cols = inputs.reshape(tok_rows, dp_count, cp_count, blk).transpose(2, 0, 1, 3)
    cols = lax.all_to_all(cols, "cp", 0, 0, tiled=True)

    both_w = jnp.concatenate([k_weight, v_weight], axis=1)
    w_rows = both_w.shape[0]
    by_dp = inputs.reshape(tok_rows, dp_count, w_rows).transpose(1, 0, 2)
    by_dp = lax.all_to_all(by_dp, "dp", 0, 0, tiled=True)
    kv_part = jnp.einsum("str,rn->stn", by_dp, both_w, preferred_element_type=jnp.float32)
    kv = reduce_over(kv_part, "dp").astype(jnp.bfloat16)
    kv_all = gather_over(kv, "cp", cp_count).reshape(seq_rows, 2 * kv_width)
    key_heads = kv_all[:, :kv_width].reshape(seq_rows, kv_heads, DH)
    value_heads = kv_all[:, kv_width:].reshape(seq_rows, kv_heads, DH)

    own_rows = lax.axis_index("cp") * tok_rows + jnp.arange(tok_rows, dtype=jnp.int32)
    own_place = place(own_rows, tok_rows, seq_rows)
    own_doc = doc_index(own_place, starts)
    key_place = place(jnp.arange(seq_rows, dtype=jnp.int32), tok_rows, seq_rows)
    key_doc = doc_index(key_place, starts)
    allowed = (key_place[None, :] <= own_place[:, None]) & (key_doc[None, :] == own_doc[:, None])

    queries = query[0].reshape(tok_rows, kv_heads, per_group, DH)
    upstream = grad_out[0].reshape(tok_rows, kv_heads, per_group, DH)

    scores = (
        jnp.einsum("qgid,kgd->giqk", queries, key_heads, preferred_element_type=jnp.float32)
        * score_scale
    )
    scores = jnp.where(allowed, scores, NEG_BIG)
    top_score = jnp.max(scores, axis=-1)
    expos = jnp.where(allowed, jnp.exp(scores - top_score[..., None]), 0.0)
    log_total = top_score + jnp.log(jnp.sum(expos, axis=-1))
    weights = jnp.where(allowed, jnp.exp(scores - log_total[..., None]), 0.0)
    weights_bf = weights.astype(jnp.bfloat16)
    out_rows = jnp.einsum(
        "giqk,kgd->qgid", weights_bf, value_heads, preferred_element_type=jnp.float32
    ).astype(jnp.bfloat16)
    delta = jnp.transpose(
        jnp.sum(upstream.astype(jnp.float32) * out_rows.astype(jnp.float32), axis=-1), (1, 2, 0)
    )
    prob_grads = jnp.einsum(
        "qgid,kgd->giqk", upstream, value_heads, preferred_element_type=jnp.float32
    )
    score_grads = (weights * (prob_grads - delta[..., None])).astype(jnp.bfloat16)
    query_acc = (
        jnp.einsum("giqk,kgd->qgid", score_grads, key_heads, preferred_element_type=jnp.float32)
        * score_scale
    )
    key_term = (
        jnp.einsum("giqk,qgid->kgd", score_grads, queries, preferred_element_type=jnp.float32)
        * score_scale
    )
    value_term = jnp.einsum(
        "giqk,qgid->kgd", weights_bf, upstream, preferred_element_type=jnp.float32
    )
    value_terms = value_term.reshape(cp_count, tok_rows, kv_width).astype(jnp.bfloat16)
    cols, value_terms = lax.optimization_barrier((cols, value_terms))
    value_grads = gather_over(reduce_over(value_terms, "cp").astype(jnp.bfloat16), "cp", cp_count)
    key_terms = key_term.reshape(cp_count, tok_rows, kv_width).astype(jnp.bfloat16)
    key_grads = gather_over(reduce_over(key_terms, "cp").astype(jnp.bfloat16), "cp", cp_count)

    value_part = jnp.einsum("ctjb,ctn->jbn", cols, value_grads, preferred_element_type=jnp.float32)
    key_part = jnp.einsum("ctjb,ctn->jbn", cols, key_grads, preferred_element_type=jnp.float32)
    result = reduce_over(jnp.concatenate([key_part, value_part], axis=2), "dp")

    attn_rows = out_rows.reshape(1, tok_rows, kv_heads * per_group * DH)
    query_rows = query_acc.astype(jnp.bfloat16).reshape(1, tok_rows, kv_heads * per_group * DH)
    return (attn_rows, query_rows, result[:, :kv_width], result[:, kv_width:])


def solution(mesh):
    placed = (
        P("dp", "cp", None),
        P("dp", "cp", "tp"),
        P("dp", "cp", "tp"),
        P("dp", "tp"),
        P("dp", "tp"),
        P("dp", None),
    )
    return jax.shard_map(
        on_device,
        mesh=mesh,
        in_specs=placed,
        out_specs=(
            P("dp", "cp", "tp"),
            P("dp", "cp", "tp"),
            P(("dp", "cp"), "tp"),
            P(("dp", "cp"), "tp"),
        ),
        check_vma=False,
    )
```

```python
import jax
import jax.numpy as jnp
from jax import lax
from jax.sharding import PartitionSpec as P

DH = 128


NEG_BIG = -1e30


def place(rows, tok_rows, seq_rows):
    stretch = rows // tok_rows
    within = rows % tok_rows
    half_rows = tok_rows // 2
    return jnp.where(
        within < half_rows,
        stretch * half_rows + within,
        seq_rows - (stretch + 1) * half_rows + within - half_rows,
    )


def doc_index(positions, starts):
    return jnp.sum((starts[None, :] <= positions[:, None]).astype(jnp.int32), axis=1) - 1


def gather_over(piece, axis, count):
    spread = jnp.broadcast_to(piece[None], (count,) + piece.shape)
    return lax.all_to_all(spread, axis, 0, 0, tiled=True)


def reduce_over(blocks, axis):
    received = lax.all_to_all(blocks, axis, 0, 0, tiled=True)
    return jnp.sum(received.astype(jnp.float32), axis=0)


def on_device(hidden, query, grad_out, k_weight, v_weight, doc_starts):
    inputs = hidden[0]
    tok_rows, width = inputs.shape
    cp_count = lax.axis_size("cp")
    dp_count = lax.axis_size("dp")
    seq_rows = tok_rows * cp_count
    score_scale = DH ** (-0.5)
    kv_width = k_weight.shape[1]
    kv_heads = kv_width // DH
    per_group = query.shape[2] // DH // kv_heads
    starts = doc_starts[0]

    blk = width // (dp_count * cp_count)
    cols = inputs.reshape(tok_rows, dp_count, cp_count, blk).transpose(2, 0, 1, 3)
    cols = lax.all_to_all(cols, "cp", 0, 0, tiled=True)

    both_w = jnp.concatenate([k_weight, v_weight], axis=1)
    w_rows = both_w.shape[0]
    by_dp = inputs.reshape(tok_rows, dp_count, w_rows).transpose(1, 0, 2)
    by_dp = lax.all_to_all(by_dp, "dp", 0, 0, tiled=True)
    kv_part = jnp.einsum("str,rn->stn", by_dp, both_w, preferred_element_type=jnp.float32)
    kv = reduce_over(kv_part, "dp").astype(jnp.bfloat16)
    key_all = gather_over(kv[:, :kv_width], "cp", cp_count)
    value_all = lax.all_gather(kv[:, kv_width:], "cp", axis=0, tiled=True)
    key_heads = key_all.reshape(seq_rows, kv_heads, DH)
    value_heads = value_all.reshape(seq_rows, kv_heads, DH)

    own_rows = lax.axis_index("cp") * tok_rows + jnp.arange(tok_rows, dtype=jnp.int32)
    own_place = place(own_rows, tok_rows, seq_rows)
    own_doc = doc_index(own_place, starts)
    key_place = place(jnp.arange(seq_rows, dtype=jnp.int32), tok_rows, seq_rows)
    key_doc = doc_index(key_place, starts)
    allowed = (key_place[None, :] <= own_place[:, None]) & (key_doc[None, :] == own_doc[:, None])

    queries = query[0].reshape(tok_rows, kv_heads, per_group, DH)
    upstream = grad_out[0].reshape(tok_rows, kv_heads, per_group, DH)

    scores = (
        jnp.einsum("qgid,kgd->giqk", queries, key_heads, preferred_element_type=jnp.float32)
        * score_scale
    )
    scores = jnp.where(allowed, scores, NEG_BIG)
    top_score = jnp.max(scores, axis=-1)
    expos = jnp.where(allowed, jnp.exp(scores - top_score[..., None]), 0.0)
    log_total = top_score + jnp.log(jnp.sum(expos, axis=-1))
    weights = jnp.where(allowed, jnp.exp(scores - log_total[..., None]), 0.0)
    weights_bf = weights.astype(jnp.bfloat16)
    out_rows = jnp.einsum(
        "giqk,kgd->qgid", weights_bf, value_heads, preferred_element_type=jnp.float32
    ).astype(jnp.bfloat16)
    delta = jnp.transpose(
        jnp.sum(upstream.astype(jnp.float32) * out_rows.astype(jnp.float32), axis=-1), (1, 2, 0)
    )
    prob_grads = jnp.einsum(
        "qgid,kgd->giqk", upstream, value_heads, preferred_element_type=jnp.float32
    )
    score_grads = (weights * (prob_grads - delta[..., None])).astype(jnp.bfloat16)
    query_acc = (
        jnp.einsum("giqk,kgd->qgid", score_grads, key_heads, preferred_element_type=jnp.float32)
        * score_scale
    )
    key_term = (
        jnp.einsum("giqk,qgid->kgd", score_grads, queries, preferred_element_type=jnp.float32)
        * score_scale
    )
    value_term = jnp.einsum(
        "giqk,qgid->kgd", weights_bf, upstream, preferred_element_type=jnp.float32
    )
    value_terms = value_term.reshape(cp_count, tok_rows, kv_width).astype(jnp.bfloat16)
    cols, value_terms = lax.optimization_barrier((cols, value_terms))
    value_grads = lax.all_gather(
        reduce_over(value_terms, "cp").astype(jnp.bfloat16), "cp", axis=0, tiled=True
    ).reshape(cp_count, tok_rows, kv_width)
    key_terms = key_term.reshape(cp_count, tok_rows, kv_width).astype(jnp.bfloat16)
    key_grads = gather_over(reduce_over(key_terms, "cp").astype(jnp.bfloat16), "cp", cp_count)

    value_part = jnp.einsum("ctjb,ctn->jbn", cols, value_grads, preferred_element_type=jnp.float32)
    key_part = jnp.einsum("ctjb,ctn->jbn", cols, key_grads, preferred_element_type=jnp.float32)
    result = reduce_over(jnp.concatenate([key_part, value_part], axis=2), "dp")

    attn_rows = out_rows.reshape(1, tok_rows, kv_heads * per_group * DH)
    query_rows = query_acc.astype(jnp.bfloat16).reshape(1, tok_rows, kv_heads * per_group * DH)
    return (attn_rows, query_rows, result[:, :kv_width], result[:, kv_width:])


def solution(mesh):
    placed = (
        P("dp", "cp", None),
        P("dp", "cp", "tp"),
        P("dp", "cp", "tp"),
        P("dp", "tp"),
        P("dp", "tp"),
        P("dp", None),
    )
    return jax.shard_map(
        on_device,
        mesh=mesh,
        in_specs=placed,
        out_specs=(
            P("dp", "cp", "tp"),
            P("dp", "cp", "tp"),
            P(("dp", "cp"), "tp"),
            P(("dp", "cp"), "tp"),
        ),
        check_vma=False,
    )
```

```python
import jax
import jax.numpy as jnp
from jax import lax
from jax.sharding import PartitionSpec as P

DH = 128


NEG_BIG = -1e30


def place(rows, tok_rows, seq_rows):
    stretch = rows // tok_rows
    within = rows % tok_rows
    half_rows = tok_rows // 2
    return jnp.where(
        within < half_rows,
        stretch * half_rows + within,
        seq_rows - (stretch + 1) * half_rows + within - half_rows,
    )


def doc_index(positions, starts):
    return jnp.sum((starts[None, :] <= positions[:, None]).astype(jnp.int32), axis=1) - 1


def gather_over(piece, axis, count):
    spread = jnp.broadcast_to(piece[None], (count,) + piece.shape)
    return lax.all_to_all(spread, axis, 0, 0, tiled=True)


def reduce_over(blocks, axis):
    received = lax.all_to_all(blocks, axis, 0, 0, tiled=True)
    return jnp.sum(received.astype(jnp.float32), axis=0)


def attend(queries, upstream, keys, values, allowed, score_scale):
    scores = (
        jnp.einsum("qid,kd->iqk", queries, keys, preferred_element_type=jnp.float32) * score_scale
    )
    scores = jnp.where(allowed, scores, NEG_BIG)
    top_score = jnp.max(scores, axis=-1)
    expos = jnp.where(allowed, jnp.exp(scores - top_score[..., None]), 0.0)
    log_total = top_score + jnp.log(jnp.sum(expos, axis=-1))
    weights = jnp.where(allowed, jnp.exp(scores - log_total[..., None]), 0.0)
    weights_bf = weights.astype(jnp.bfloat16)
    out_rows = jnp.einsum(
        "iqk,kd->qid", weights_bf, values, preferred_element_type=jnp.float32
    ).astype(jnp.bfloat16)
    delta = jnp.transpose(
        jnp.sum(upstream.astype(jnp.float32) * out_rows.astype(jnp.float32), axis=-1), (1, 0)
    )
    prob_grads = jnp.einsum("qid,kd->iqk", upstream, values, preferred_element_type=jnp.float32)
    score_grads = (weights * (prob_grads - delta[..., None])).astype(jnp.bfloat16)
    query_grad = (
        jnp.einsum("iqk,kd->qid", score_grads, keys, preferred_element_type=jnp.float32)
        * score_scale
    ).astype(jnp.bfloat16)
    key_term = (
        jnp.einsum("iqk,qid->kd", score_grads, queries, preferred_element_type=jnp.float32)
        * score_scale
    )
    value_term = jnp.einsum("iqk,qid->kd", weights_bf, upstream, preferred_element_type=jnp.float32)
    return out_rows, query_grad, key_term, value_term


def on_device(hidden, query, grad_out, k_weight, v_weight, doc_starts):
    inputs = hidden[0]
    tok_rows, width = inputs.shape
    cp_count = lax.axis_size("cp")
    dp_count = lax.axis_size("dp")
    seq_rows = tok_rows * cp_count
    score_scale = DH ** (-0.5)
    kv_width = k_weight.shape[1]
    kv_heads = kv_width // DH
    per_group = query.shape[2] // DH // kv_heads
    starts = doc_starts[0]

    blk = width // (dp_count * cp_count)
    cols = inputs.reshape(tok_rows, dp_count, cp_count, blk).transpose(2, 0, 1, 3)
    cols = lax.all_to_all(cols, "cp", 0, 0, tiled=True)

    both_w = jnp.concatenate([k_weight, v_weight], axis=1)
    w_rows = both_w.shape[0]
    by_dp = inputs.reshape(tok_rows, dp_count, w_rows).transpose(1, 0, 2)
    by_dp = lax.all_to_all(by_dp, "dp", 0, 0, tiled=True)
    kv_part = jnp.einsum("str,rn->stn", by_dp, both_w, preferred_element_type=jnp.float32)
    kv = reduce_over(kv_part, "dp").astype(jnp.bfloat16)

    own_rows = lax.axis_index("cp") * tok_rows + jnp.arange(tok_rows, dtype=jnp.int32)
    own_place = place(own_rows, tok_rows, seq_rows)
    own_doc = doc_index(own_place, starts)
    key_place = place(jnp.arange(seq_rows, dtype=jnp.int32), tok_rows, seq_rows)
    key_doc = doc_index(key_place, starts)
    allowed = (key_place[None, :] <= own_place[:, None]) & (key_doc[None, :] == own_doc[:, None])

    queries = query[0].reshape(tok_rows, kv_heads, per_group, DH)
    upstream = grad_out[0].reshape(tok_rows, kv_heads, per_group, DH)

    outs, qgrads, key_parts, value_parts = [], [], [], []
    for head in range(kv_heads):
        head_kv = jnp.concatenate(
            [kv[:, head * DH:(head + 1) * DH], kv[:, kv_width + head * DH:kv_width + (head + 1) * DH]],
            axis=1,
        )
        head_kv = gather_over(head_kv, "cp", cp_count).reshape(seq_rows, 2 * DH)
        head_out, head_qgrad, key_term, value_term = attend(
            queries[:, head], upstream[:, head], head_kv[:, :DH], head_kv[:, DH:], allowed, score_scale
        )
        outs.append(head_out)
        qgrads.append(head_qgrad)
        terms = jnp.concatenate([key_term, value_term], axis=1)
        terms = terms.reshape(cp_count, tok_rows, 2 * DH).astype(jnp.bfloat16)
        if head == 0:
            cols, terms = lax.optimization_barrier((cols, terms))
        head_grads = gather_over(reduce_over(terms, "cp").astype(jnp.bfloat16), "cp", cp_count)
        key_parts.append(head_grads[..., :DH])
        value_parts.append(head_grads[..., DH:])
    out_rows = jnp.stack(outs, axis=1)
    query_acc = jnp.stack(qgrads, axis=1)
    key_grads = jnp.concatenate(key_parts, axis=2)
    value_grads = jnp.concatenate(value_parts, axis=2)

    value_part = jnp.einsum("ctjb,ctn->jbn", cols, value_grads, preferred_element_type=jnp.float32)
    key_part = jnp.einsum("ctjb,ctn->jbn", cols, key_grads, preferred_element_type=jnp.float32)
    result = reduce_over(jnp.concatenate([key_part, value_part], axis=2), "dp")

    attn_rows = out_rows.reshape(1, tok_rows, kv_heads * per_group * DH)
    query_rows = query_acc.reshape(1, tok_rows, kv_heads * per_group * DH)
    return (attn_rows, query_rows, result[:, :kv_width], result[:, kv_width:])


def solution(mesh):
    placed = (
        P("dp", "cp", None),
        P("dp", "cp", "tp"),
        P("dp", "cp", "tp"),
        P("dp", "tp"),
        P("dp", "tp"),
        P("dp", None),
    )
    return jax.shard_map(
        on_device,
        mesh=mesh,
        in_specs=placed,
        out_specs=(
            P("dp", "cp", "tp"),
            P("dp", "cp", "tp"),
            P(("dp", "cp"), "tp"),
            P(("dp", "cp"), "tp"),
        ),
        check_vma=False,
    )
```

```python
import jax
import jax.numpy as jnp
from jax import lax
from jax.sharding import PartitionSpec as P

DH = 128


NEG_BIG = -1e30


def place(rows, tok_rows, seq_rows):
    stretch = rows // tok_rows
    within = rows % tok_rows
    half_rows = tok_rows // 2
    return jnp.where(
        within < half_rows,
        stretch * half_rows + within,
        seq_rows - (stretch + 1) * half_rows + within - half_rows,
    )


def doc_index(positions, starts):
    return jnp.sum((starts[None, :] <= positions[:, None]).astype(jnp.int32), axis=1) - 1


def gather_over(piece, axis, count):
    spread = jnp.broadcast_to(piece[None], (count,) + piece.shape)
    return lax.all_to_all(spread, axis, 0, 0, tiled=True)


def reduce_over(blocks, axis):
    received = lax.all_to_all(blocks, axis, 0, 0, tiled=True)
    return jnp.sum(received.astype(jnp.float32), axis=0)


def on_device(hidden, query, grad_out, k_weight, v_weight, doc_starts):
    inputs = hidden[0]
    tok_rows, width = inputs.shape
    cp_count = lax.axis_size("cp")
    dp_count = lax.axis_size("dp")
    seq_rows = tok_rows * cp_count
    score_scale = DH ** (-0.5)
    kv_width = k_weight.shape[1]
    kv_heads = kv_width // DH
    per_group = query.shape[2] // DH // kv_heads
    starts = doc_starts[0]

    blk = width // (dp_count * cp_count)
    tp_count = lax.axis_size("tp")
    quarter = tok_rows // tp_count
    my_rows = lax.dynamic_slice_in_dim(inputs, lax.axis_index("tp") * quarter, quarter, 0)
    cols = my_rows.reshape(quarter, dp_count, cp_count, blk).transpose(2, 0, 1, 3)
    cols = lax.all_to_all(cols, "cp", 0, 0, tiled=True)

    both_w = jnp.concatenate([k_weight, v_weight], axis=1)
    w_rows = both_w.shape[0]
    by_dp = inputs.reshape(tok_rows, dp_count, w_rows).transpose(1, 0, 2)
    by_dp = lax.all_to_all(by_dp, "dp", 0, 0, tiled=True)
    kv_part = jnp.einsum("str,rn->stn", by_dp, both_w, preferred_element_type=jnp.float32)
    kv = reduce_over(kv_part, "dp").astype(jnp.bfloat16)
    kv_all = gather_over(kv, "cp", cp_count).reshape(seq_rows, 2 * kv_width)
    key_heads = kv_all[:, :kv_width].reshape(seq_rows, kv_heads, DH)
    value_heads = kv_all[:, kv_width:].reshape(seq_rows, kv_heads, DH)

    own_rows = lax.axis_index("cp") * tok_rows + jnp.arange(tok_rows, dtype=jnp.int32)
    own_place = place(own_rows, tok_rows, seq_rows)
    own_doc = doc_index(own_place, starts)
    key_place = place(jnp.arange(seq_rows, dtype=jnp.int32), tok_rows, seq_rows)
    key_doc = doc_index(key_place, starts)
    allowed = (key_place[None, :] <= own_place[:, None]) & (key_doc[None, :] == own_doc[:, None])

    queries = query[0].reshape(tok_rows, kv_heads, per_group, DH)
    upstream = grad_out[0].reshape(tok_rows, kv_heads, per_group, DH)

    scores = (
        jnp.einsum("qgid,kgd->giqk", queries, key_heads, preferred_element_type=jnp.float32)
        * score_scale
    )
    scores = jnp.where(allowed, scores, NEG_BIG)
    top_score = jnp.max(scores, axis=-1)
    expos = jnp.where(allowed, jnp.exp(scores - top_score[..., None]), 0.0)
    log_total = top_score + jnp.log(jnp.sum(expos, axis=-1))
    weights = jnp.where(allowed, jnp.exp(scores - log_total[..., None]), 0.0)
    weights_bf = weights.astype(jnp.bfloat16)
    out_rows = jnp.einsum(
        "giqk,kgd->qgid", weights_bf, value_heads, preferred_element_type=jnp.float32
    ).astype(jnp.bfloat16)
    delta = jnp.transpose(
        jnp.sum(upstream.astype(jnp.float32) * out_rows.astype(jnp.float32), axis=-1), (1, 2, 0)
    )
    prob_grads = jnp.einsum(
        "qgid,kgd->giqk", upstream, value_heads, preferred_element_type=jnp.float32
    )
    score_grads = (weights * (prob_grads - delta[..., None])).astype(jnp.bfloat16)
    query_acc = (
        jnp.einsum("giqk,kgd->qgid", score_grads, key_heads, preferred_element_type=jnp.float32)
        * score_scale
    )
    key_term = (
        jnp.einsum("giqk,qgid->kgd", score_grads, queries, preferred_element_type=jnp.float32)
        * score_scale
    )
    value_term = jnp.einsum(
        "giqk,qgid->kgd", weights_bf, upstream, preferred_element_type=jnp.float32
    )
    value_terms = value_term.reshape(cp_count, tok_rows, kv_width).astype(jnp.bfloat16)
    cols, value_terms = lax.optimization_barrier((cols, value_terms))
    cols = lax.all_gather(cols, "tp", axis=1, tiled=True)
    value_grads = gather_over(reduce_over(value_terms, "cp").astype(jnp.bfloat16), "cp", cp_count)
    key_terms = key_term.reshape(cp_count, tok_rows, kv_width).astype(jnp.bfloat16)
    key_grads = gather_over(reduce_over(key_terms, "cp").astype(jnp.bfloat16), "cp", cp_count)

    value_part = jnp.einsum("ctjb,ctn->jbn", cols, value_grads, preferred_element_type=jnp.float32)
    key_part = jnp.einsum("ctjb,ctn->jbn", cols, key_grads, preferred_element_type=jnp.float32)
    result = reduce_over(jnp.concatenate([key_part, value_part], axis=2), "dp")

    attn_rows = out_rows.reshape(1, tok_rows, kv_heads * per_group * DH)
    query_rows = query_acc.astype(jnp.bfloat16).reshape(1, tok_rows, kv_heads * per_group * DH)
    return (attn_rows, query_rows, result[:, :kv_width], result[:, kv_width:])


def solution(mesh):
    placed = (
        P("dp", "cp", None),
        P("dp", "cp", "tp"),
        P("dp", "cp", "tp"),
        P("dp", "tp"),
        P("dp", "tp"),
        P("dp", None),
    )
    return jax.shard_map(
        on_device,
        mesh=mesh,
        in_specs=placed,
        out_specs=(
            P("dp", "cp", "tp"),
            P("dp", "cp", "tp"),
            P(("dp", "cp"), "tp"),
            P(("dp", "cp"), "tp"),
        ),
        check_vma=False,
    )
```

```python
import jax
import jax.numpy as jnp
from jax import lax
from jax.sharding import PartitionSpec as P

DH = 128


NEG_BIG = -1e30


def place(rows, tok_rows, seq_rows):
    stretch = rows // tok_rows
    within = rows % tok_rows
    half_rows = tok_rows // 2
    return jnp.where(
        within < half_rows,
        stretch * half_rows + within,
        seq_rows - (stretch + 1) * half_rows + within - half_rows,
    )


def doc_index(positions, starts):
    return jnp.sum((starts[None, :] <= positions[:, None]).astype(jnp.int32), axis=1) - 1


def gather_over(piece, axis, count):
    spread = jnp.broadcast_to(piece[None], (count,) + piece.shape)
    return lax.all_to_all(spread, axis, 0, 0, tiled=True)


def reduce_over(blocks, axis):
    received = lax.all_to_all(blocks, axis, 0, 0, tiled=True)
    return jnp.sum(received.astype(jnp.float32), axis=0)


def on_device(hidden, query, grad_out, k_weight, v_weight, doc_starts):
    inputs = hidden[0]
    tok_rows, width = inputs.shape
    cp_count = lax.axis_size("cp")
    dp_count = lax.axis_size("dp")
    seq_rows = tok_rows * cp_count
    score_scale = DH ** (-0.5)
    kv_width = k_weight.shape[1]
    kv_heads = kv_width // DH
    per_group = query.shape[2] // DH // kv_heads
    starts = doc_starts[0]

    blk = width // (dp_count * cp_count)
    tp_count = lax.axis_size("tp")
    quarter = tok_rows // tp_count
    my_rows = lax.dynamic_slice_in_dim(inputs, lax.axis_index("tp") * quarter, quarter, 0)
    cols = my_rows.reshape(quarter, dp_count, cp_count, blk).transpose(2, 0, 1, 3)
    cols = lax.all_to_all(cols, "cp", 0, 0, tiled=True)

    both_w = jnp.concatenate([k_weight, v_weight], axis=1)
    w_rows = both_w.shape[0]
    by_dp = inputs.reshape(tok_rows, dp_count, w_rows).transpose(1, 0, 2)
    by_dp = lax.all_to_all(by_dp, "dp", 0, 0, tiled=True)
    kv_part = jnp.einsum("str,rn->stn", by_dp, both_w, preferred_element_type=jnp.float32)
    kv = reduce_over(kv_part, "dp").astype(jnp.bfloat16)
    kv_all = gather_over(kv, "cp", cp_count).reshape(seq_rows, 2 * kv_width)
    key_heads = kv_all[:, :kv_width].reshape(seq_rows, kv_heads, DH)
    value_heads = kv_all[:, kv_width:].reshape(seq_rows, kv_heads, DH)

    own_rows = lax.axis_index("cp") * tok_rows + jnp.arange(tok_rows, dtype=jnp.int32)
    own_place = place(own_rows, tok_rows, seq_rows)
    own_doc = doc_index(own_place, starts)
    key_place = place(jnp.arange(seq_rows, dtype=jnp.int32), tok_rows, seq_rows)
    key_doc = doc_index(key_place, starts)
    allowed = (key_place[None, :] <= own_place[:, None]) & (key_doc[None, :] == own_doc[:, None])

    queries = query[0].reshape(tok_rows, kv_heads, per_group, DH)
    upstream = grad_out[0].reshape(tok_rows, kv_heads, per_group, DH)

    scores = (
        jnp.einsum("qgid,kgd->giqk", queries, key_heads, preferred_element_type=jnp.float32)
        * score_scale
    )
    scores = jnp.where(allowed, scores, NEG_BIG)
    top_score = jnp.max(scores, axis=-1)
    expos = jnp.where(allowed, jnp.exp(scores - top_score[..., None]), 0.0)
    log_total = top_score + jnp.log(jnp.sum(expos, axis=-1))
    weights = jnp.where(allowed, jnp.exp(scores - log_total[..., None]), 0.0)
    weights_bf = weights.astype(jnp.bfloat16)
    out_rows = jnp.einsum(
        "giqk,kgd->qgid", weights_bf, value_heads, preferred_element_type=jnp.float32
    ).astype(jnp.bfloat16)
    delta = jnp.transpose(
        jnp.sum(upstream.astype(jnp.float32) * out_rows.astype(jnp.float32), axis=-1), (1, 2, 0)
    )
    prob_grads = jnp.einsum(
        "qgid,kgd->giqk", upstream, value_heads, preferred_element_type=jnp.float32
    )
    score_grads = (weights * (prob_grads - delta[..., None])).astype(jnp.bfloat16)
    query_acc = (
        jnp.einsum("giqk,kgd->qgid", score_grads, key_heads, preferred_element_type=jnp.float32)
        * score_scale
    )
    key_term = (
        jnp.einsum("giqk,qgid->kgd", score_grads, queries, preferred_element_type=jnp.float32)
        * score_scale
    )
    value_term = jnp.einsum(
        "giqk,qgid->kgd", weights_bf, upstream, preferred_element_type=jnp.float32
    )
    value_terms = value_term.reshape(cp_count, tok_rows, kv_width).astype(jnp.bfloat16)
    cols, value_terms = lax.optimization_barrier((cols, value_terms))
    cols = gather_over(cols, "tp", tp_count)
    cols = jnp.moveaxis(cols, 0, 1).reshape(cp_count, tok_rows, dp_count, blk)
    value_own = reduce_over(value_terms, "cp").astype(jnp.bfloat16)
    key_terms = key_term.reshape(cp_count, tok_rows, kv_width).astype(jnp.bfloat16)
    mixed = jnp.concatenate(
        [jnp.broadcast_to(value_own[None], (cp_count, tok_rows, kv_width)), key_terms], axis=2
    )
    mixed = lax.all_to_all(mixed, "cp", 0, 0, tiled=True)
    value_grads = mixed[..., :kv_width]
    key_own = jnp.sum(mixed[..., kv_width:].astype(jnp.float32), axis=0).astype(jnp.bfloat16)
    key_grads = gather_over(key_own, "cp", cp_count)

    value_part = jnp.einsum("ctjb,ctn->jbn", cols, value_grads, preferred_element_type=jnp.float32)
    key_part = jnp.einsum("ctjb,ctn->jbn", cols, key_grads, preferred_element_type=jnp.float32)
    result = reduce_over(jnp.concatenate([key_part, value_part], axis=2), "dp")

    attn_rows = out_rows.reshape(1, tok_rows, kv_heads * per_group * DH)
    query_rows = query_acc.astype(jnp.bfloat16).reshape(1, tok_rows, kv_heads * per_group * DH)
    return (attn_rows, query_rows, result[:, :kv_width], result[:, kv_width:])


def solution(mesh):
    placed = (
        P("dp", "cp", None),
        P("dp", "cp", "tp"),
        P("dp", "cp", "tp"),
        P("dp", "tp"),
        P("dp", "tp"),
        P("dp", None),
    )
    return jax.shard_map(
        on_device,
        mesh=mesh,
        in_specs=placed,
        out_specs=(
            P("dp", "cp", "tp"),
            P("dp", "cp", "tp"),
            P(("dp", "cp"), "tp"),
            P(("dp", "cp"), "tp"),
        ),
        check_vma=False,
    )
```

```python
import jax
import jax.numpy as jnp
from jax import lax
from jax.sharding import PartitionSpec as P

DH = 128


NEG_BIG = -1e30


def place(rows, tok_rows, seq_rows):
    stretch = rows // tok_rows
    within = rows % tok_rows
    half_rows = tok_rows // 2
    return jnp.where(
        within < half_rows,
        stretch * half_rows + within,
        seq_rows - (stretch + 1) * half_rows + within - half_rows,
    )


def doc_index(positions, starts):
    return jnp.sum((starts[None, :] <= positions[:, None]).astype(jnp.int32), axis=1) - 1


def gather_over(piece, axis, count):
    spread = jnp.broadcast_to(piece[None], (count,) + piece.shape)
    return lax.all_to_all(spread, axis, 0, 0, tiled=True)


def reduce_over(blocks, axis):
    received = lax.all_to_all(blocks, axis, 0, 0, tiled=True)
    return jnp.sum(received.astype(jnp.float32), axis=0)


def on_device(hidden, query, grad_out, k_weight, v_weight, doc_starts):
    inputs = hidden[0]
    tok_rows, width = inputs.shape
    cp_count = lax.axis_size("cp")
    dp_count = lax.axis_size("dp")
    seq_rows = tok_rows * cp_count
    score_scale = DH ** (-0.5)
    kv_width = k_weight.shape[1]
    kv_heads = kv_width // DH
    per_group = query.shape[2] // DH // kv_heads
    starts = doc_starts[0]

    blk = width // (dp_count * cp_count)
    cp_index = lax.axis_index("cp")
    to_send = inputs.reshape(tok_rows, dp_count, cp_count, blk).transpose(2, 0, 1, 3)
    pieces = [lax.dynamic_index_in_dim(to_send, cp_index, 0, keepdims=False)]
    for shift in range(1, cp_count):
        block = lax.dynamic_index_in_dim(to_send, (cp_index + shift) % cp_count, 0, keepdims=False)
        pairs = [(i, (i + shift) % cp_count) for i in range(cp_count)]
        pieces.append(lax.ppermute(block, "cp", pairs))
    cols = jnp.roll(jnp.stack(pieces[::-1]), cp_index + 1, axis=0)

    both_w = jnp.concatenate([k_weight, v_weight], axis=1)
    w_rows = both_w.shape[0]
    by_dp = inputs.reshape(tok_rows, dp_count, w_rows).transpose(1, 0, 2)
    by_dp = lax.all_to_all(by_dp, "dp", 0, 0, tiled=True)
    kv_part = jnp.einsum("str,rn->stn", by_dp, both_w, preferred_element_type=jnp.float32)
    kv = reduce_over(kv_part, "dp").astype(jnp.bfloat16)
    kv_all = gather_over(kv, "cp", cp_count).reshape(seq_rows, 2 * kv_width)
    key_heads = kv_all[:, :kv_width].reshape(seq_rows, kv_heads, DH)
    value_heads = kv_all[:, kv_width:].reshape(seq_rows, kv_heads, DH)

    own_rows = lax.axis_index("cp") * tok_rows + jnp.arange(tok_rows, dtype=jnp.int32)
    own_place = place(own_rows, tok_rows, seq_rows)
    own_doc = doc_index(own_place, starts)
    key_place = place(jnp.arange(seq_rows, dtype=jnp.int32), tok_rows, seq_rows)
    key_doc = doc_index(key_place, starts)
    allowed = (key_place[None, :] <= own_place[:, None]) & (key_doc[None, :] == own_doc[:, None])

    queries = query[0].reshape(tok_rows, kv_heads, per_group, DH)
    upstream = grad_out[0].reshape(tok_rows, kv_heads, per_group, DH)

    scores = (
        jnp.einsum("qgid,kgd->giqk", queries, key_heads, preferred_element_type=jnp.float32)
        * score_scale
    )
    scores = jnp.where(allowed, scores, NEG_BIG)
    top_score = jnp.max(scores, axis=-1)
    expos = jnp.where(allowed, jnp.exp(scores - top_score[..., None]), 0.0)
    log_total = top_score + jnp.log(jnp.sum(expos, axis=-1))
    weights = jnp.where(allowed, jnp.exp(scores - log_total[..., None]), 0.0)
    weights_bf = weights.astype(jnp.bfloat16)
    out_rows = jnp.einsum(
        "giqk,kgd->qgid", weights_bf, value_heads, preferred_element_type=jnp.float32
    ).astype(jnp.bfloat16)
    delta = jnp.transpose(
        jnp.sum(upstream.astype(jnp.float32) * out_rows.astype(jnp.float32), axis=-1), (1, 2, 0)
    )
    prob_grads = jnp.einsum(
        "qgid,kgd->giqk", upstream, value_heads, preferred_element_type=jnp.float32
    )
    score_grads = (weights * (prob_grads - delta[..., None])).astype(jnp.bfloat16)
    query_acc = (
        jnp.einsum("giqk,kgd->qgid", score_grads, key_heads, preferred_element_type=jnp.float32)
        * score_scale
    )
    key_term = (
        jnp.einsum("giqk,qgid->kgd", score_grads, queries, preferred_element_type=jnp.float32)
        * score_scale
    )
    value_term = jnp.einsum(
        "giqk,qgid->kgd", weights_bf, upstream, preferred_element_type=jnp.float32
    )
    value_terms = value_term.reshape(cp_count, tok_rows, kv_width).astype(jnp.bfloat16)
    cols, value_terms = lax.optimization_barrier((cols, value_terms))
    value_grads = gather_over(reduce_over(value_terms, "cp").astype(jnp.bfloat16), "cp", cp_count)
    key_terms = key_term.reshape(cp_count, tok_rows, kv_width).astype(jnp.bfloat16)
    key_grads = gather_over(reduce_over(key_terms, "cp").astype(jnp.bfloat16), "cp", cp_count)

    value_part = jnp.einsum("ctjb,ctn->jbn", cols, value_grads, preferred_element_type=jnp.float32)
    key_part = jnp.einsum("ctjb,ctn->jbn", cols, key_grads, preferred_element_type=jnp.float32)
    result = reduce_over(jnp.concatenate([key_part, value_part], axis=2), "dp")

    attn_rows = out_rows.reshape(1, tok_rows, kv_heads * per_group * DH)
    query_rows = query_acc.astype(jnp.bfloat16).reshape(1, tok_rows, kv_heads * per_group * DH)
    return (attn_rows, query_rows, result[:, :kv_width], result[:, kv_width:])


def solution(mesh):
    placed = (
        P("dp", "cp", None),
        P("dp", "cp", "tp"),
        P("dp", "cp", "tp"),
        P("dp", "tp"),
        P("dp", "tp"),
        P("dp", None),
    )
    return jax.shard_map(
        on_device,
        mesh=mesh,
        in_specs=placed,
        out_specs=(
            P("dp", "cp", "tp"),
            P("dp", "cp", "tp"),
            P(("dp", "cp"), "tp"),
            P(("dp", "cp"), "tp"),
        ),
        check_vma=False,
    )
```

```python
import jax
import jax.numpy as jnp
from jax import lax
from jax.sharding import PartitionSpec as P

DH = 128


NEG_BIG = -1e30


def place(rows, tok_rows, seq_rows):
    stretch = rows // tok_rows
    within = rows % tok_rows
    half_rows = tok_rows // 2
    return jnp.where(
        within < half_rows,
        stretch * half_rows + within,
        seq_rows - (stretch + 1) * half_rows + within - half_rows,
    )


def doc_index(positions, starts):
    return jnp.sum((starts[None, :] <= positions[:, None]).astype(jnp.int32), axis=1) - 1


def gather_over(piece, axis, count):
    spread = jnp.broadcast_to(piece[None], (count,) + piece.shape)
    return lax.all_to_all(spread, axis, 0, 0, tiled=True)


def reduce_over(blocks, axis):
    received = lax.all_to_all(blocks, axis, 0, 0, tiled=True)
    return jnp.sum(received.astype(jnp.float32), axis=0)


def on_device(hidden, query, grad_out, k_weight, v_weight, doc_starts):
    inputs = hidden[0]
    tok_rows, width = inputs.shape
    cp_count = lax.axis_size("cp")
    dp_count = lax.axis_size("dp")
    seq_rows = tok_rows * cp_count
    score_scale = DH ** (-0.5)
    kv_width = k_weight.shape[1]
    kv_heads = kv_width // DH
    per_group = query.shape[2] // DH // kv_heads
    starts = doc_starts[0]

    blk = width // (dp_count * cp_count)
    cols = inputs.reshape(tok_rows, dp_count, cp_count, blk).transpose(2, 0, 1, 3)
    cols = lax.all_to_all(cols, "cp", 0, 0, tiled=True)

    both_w = jnp.concatenate([k_weight, v_weight], axis=1)
    w_rows = both_w.shape[0]
    by_dp = inputs.reshape(tok_rows, dp_count, w_rows).transpose(1, 0, 2)
    by_dp = lax.all_to_all(by_dp, "dp", 0, 0, tiled=True)
    kv_part = jnp.einsum("str,rn->stn", by_dp, both_w, preferred_element_type=jnp.float32)
    kv = reduce_over(kv_part, "dp").astype(jnp.bfloat16)
    kv_all = gather_over(kv, "cp", cp_count).reshape(seq_rows, 2 * kv_width)
    key_heads = kv_all[:, :kv_width].reshape(seq_rows, kv_heads, DH)
    value_heads = kv_all[:, kv_width:].reshape(seq_rows, kv_heads, DH)

    own_rows = lax.axis_index("cp") * tok_rows + jnp.arange(tok_rows, dtype=jnp.int32)
    own_place = place(own_rows, tok_rows, seq_rows)
    own_doc = doc_index(own_place, starts)
    key_place = place(jnp.arange(seq_rows, dtype=jnp.int32), tok_rows, seq_rows)
    key_doc = doc_index(key_place, starts)
    allowed = (key_place[None, :] <= own_place[:, None]) & (key_doc[None, :] == own_doc[:, None])

    queries = query[0].reshape(tok_rows, kv_heads, per_group, DH)
    upstream = grad_out[0].reshape(tok_rows, kv_heads, per_group, DH)

    scores = (
        jnp.einsum("qgid,kgd->giqk", queries, key_heads, preferred_element_type=jnp.float32)
        * score_scale
    )
    scores = jnp.where(allowed, scores, NEG_BIG)
    top_score = jnp.max(scores, axis=-1)
    expos = jnp.where(allowed, jnp.exp(scores - top_score[..., None]), 0.0)
    log_total = top_score + jnp.log(jnp.sum(expos, axis=-1))
    weights = jnp.where(allowed, jnp.exp(scores - log_total[..., None]), 0.0)
    weights_bf = weights.astype(jnp.bfloat16)
    out_rows = jnp.einsum(
        "giqk,kgd->qgid", weights_bf, value_heads, preferred_element_type=jnp.float32
    ).astype(jnp.bfloat16)
    delta = jnp.transpose(
        jnp.sum(upstream.astype(jnp.float32) * out_rows.astype(jnp.float32), axis=-1), (1, 2, 0)
    )
    prob_grads = jnp.einsum(
        "qgid,kgd->giqk", upstream, value_heads, preferred_element_type=jnp.float32
    )
    score_grads = (weights * (prob_grads - delta[..., None])).astype(jnp.bfloat16)
    query_acc = (
        jnp.einsum("giqk,kgd->qgid", score_grads, key_heads, preferred_element_type=jnp.float32)
        * score_scale
    )
    key_term = (
        jnp.einsum("giqk,qgid->kgd", score_grads, queries, preferred_element_type=jnp.float32)
        * score_scale
    )
    value_term = jnp.einsum(
        "giqk,qgid->kgd", weights_bf, upstream, preferred_element_type=jnp.float32
    )
    value_terms = value_term.reshape(cp_count, tok_rows, kv_width).astype(jnp.bfloat16)
    cols, value_terms = lax.optimization_barrier((cols, value_terms))
    value_own = reduce_over(value_terms, "cp").astype(jnp.bfloat16)
    key_terms = key_term.reshape(cp_count, tok_rows, kv_width).astype(jnp.bfloat16)
    mixed = jnp.concatenate(
        [jnp.broadcast_to(value_own[None], (cp_count, tok_rows, kv_width)), key_terms], axis=2
    )
    mixed = lax.all_to_all(mixed, "cp", 0, 0, tiled=True)
    value_grads = mixed[..., :kv_width]
    key_own = jnp.sum(mixed[..., kv_width:].astype(jnp.float32), axis=0).astype(jnp.bfloat16)
    key_grads = gather_over(key_own, "cp", cp_count)

    value_part = jnp.einsum("ctjb,ctn->jbn", cols, value_grads, preferred_element_type=jnp.float32)
    key_part = jnp.einsum("ctjb,ctn->jbn", cols, key_grads, preferred_element_type=jnp.float32)
    result = reduce_over(jnp.concatenate([key_part, value_part], axis=2), "dp")

    attn_rows = out_rows.reshape(1, tok_rows, kv_heads * per_group * DH)
    query_rows = query_acc.astype(jnp.bfloat16).reshape(1, tok_rows, kv_heads * per_group * DH)
    return (attn_rows, query_rows, result[:, :kv_width], result[:, kv_width:])


def solution(mesh):
    placed = (
        P("dp", "cp", None),
        P("dp", "cp", "tp"),
        P("dp", "cp", "tp"),
        P("dp", "tp"),
        P("dp", "tp"),
        P("dp", None),
    )
    return jax.shard_map(
        on_device,
        mesh=mesh,
        in_specs=placed,
        out_specs=(
            P("dp", "cp", "tp"),
            P("dp", "cp", "tp"),
            P(("dp", "cp"), "tp"),
            P(("dp", "cp"), "tp"),
        ),
        check_vma=False,
    )
```
